256 devices in a mesh: tok: 32 (over z, x), head: 8 (over y, core).
Axes of the slice: x: 4, y: 4, z: 8, core: 2. Of those that a mesh axis runs over, the one named last changes fastest.
Arguments:
- embeddings: bfloat16 [4096, 4096], P('tok'), may hold values from -6 to 6
- norm_gain: bfloat16 [4096], replicated, may hold values from 0.099609375 to 1.8984375
- query_key_value_weight: bfloat16 [4096, 6144], P(None, 'head'), may hold values from -0.09375 to 0.09375
- embed_table: bfloat16 [65536, 4096], P('tok', 'head'), may hold values from -6 to 6
- rotated_cache_pages: bfloat16 [32, 32, 256, 2048], P('tok', None, None, 'head'), may hold values from -300 to 300
- page_owner_device: int32 [32, 32], P('tok'), may hold values from 0 to 31, each once within a row
- cached_length: int32 [32], P('tok'), may hold values from 2 to 8192, as said below
- vocab_shard: int32 [4096, 1], P('tok'), may hold values from 0 to 31; in each aligned block of 128 rows (0 to 127, 128 to 255, ...) at most 8 rows name the same one
- shard_row: int32 [4096], P('tok'), may hold values from 0 to 2047
- accept: int32 [4096], P('tok'), may hold values from 0 to 1, as said below
Outputs:
- out_first: bfloat16 [4096, 4096], P('tok', 'head')
- out_second: bfloat16 [4096, 4096], P('tok', 'head')
The draws below stay inside these ranges and needn't reach their ends.
Inputs may be any that keep to these rules, and one draw needn't show every extreme that they name: `page_owner_device`: each row names every device of the tok axis once. `cached_length`: some request has exactly 8192 cached positions. `vocab_shard`: at most 8 of the 128 tokens of one request name the same shard, and some shard is named that often. `accept`: at most 32 accepted tokens in one request's block; some block has exactly 32.
All inputs are finite; a program needn't handle non-finite values.
Results may differ from the reference program's by a relative error of at most 0.017.
The reference program's roundings to bfloat16 on the way count: a program that leaves them out, or rounds other values in their place, can miss the bound.
Values may be sent and summed in bfloat16 or wider, within the bound.
No kernel may reach another device: no remote copies, remote signals or barrier semaphores. Data moves between devices by JAX's collectives and lax.ppermute only.
A program may use at most 128 MiB of HBM per device.

```python
import math
import jax
import jax.numpy as jnp
import numpy as np
from jax import lax

MODEL_WIDTH = 4096
QUERY_HEADS = 32
KEY_VALUE_HEADS = 8
HEAD_SIZE = 128
VOCAB = 65536
BLOCK_TOKENS = 128
PAGE_POSITIONS = 256
REQUEST_COUNT = 32
TOKENS = 4096
CAP = 8
ACC = 32
SHARD_ROWS = 2048


def draw_rotated_cache_pages(key, part):
    key_first = jax.random.fold_in(key, 0)
    complete_shape = (REQUEST_COUNT, REQUEST_COUNT, PAGE_POSITIONS, KEY_VALUE_HEADS, 2, HEAD_SIZE)
    gaussian_draw = jnp.clip(jax.random.normal(key_first, complete_shape, jnp.float32), -6.0, 6.0)
    return gaussian_draw.reshape(REQUEST_COUNT, REQUEST_COUNT, PAGE_POSITIONS, KEY_VALUE_HEADS * 2 * HEAD_SIZE).astype(jnp.bfloat16)


def draw_cached_length(key, part):
    key_first, key_second = jax.random.split(key)
    longest = PAGE_POSITIONS * REQUEST_COUNT
    lengths = jax.random.randint(key_first, (REQUEST_COUNT,), 2, longest + 1)
    chosen = jax.random.randint(key_second, (), 0, REQUEST_COUNT)
    return jnp.where(jnp.arange(REQUEST_COUNT) == chosen, longest, lengths).astype(jnp.int32)


def draw_accept(key, part):
    key_first, key_second, key_slice_three = jax.random.split(key, 3)
    counts = jax.random.randint(key_first, (REQUEST_COUNT,), max(ACC // 2, 1), ACC + 1)
    chosen = jax.random.randint(key_second, (), 0, REQUEST_COUNT)
    counts = jnp.where(jnp.arange(REQUEST_COUNT) == chosen, ACC, counts)
    scores = jax.random.randint(key_slice_three, (REQUEST_COUNT, BLOCK_TOKENS), 0, 1048576) * BLOCK_TOKENS + jnp.arange(BLOCK_TOKENS)[None, :]
    ranking = jnp.argsort(jnp.argsort(scores, axis=1), axis=1)
    return (ranking < counts[:, None]).astype(jnp.int32).reshape(TOKENS)


def with_ends(values, rng, smallest, top_value):
    longest = values.shape.index(max(values.shape))
    spots = []
    for shift in (0, 1):
        where = [jax.random.randint(jax.random.fold_in(rng, axis), (), 0, length) for axis, length in enumerate(values.shape)]
        where[longest] = (where[longest] + shift) % values.shape[longest]
        spots.append(tuple(where))
    return values.at[spots[0]].set(smallest).at[spots[1]].set(top_value)


def steps_of(rng, shape, pieces, least, top_value):
    factor_of = 1.0
    for axis_at, blocks in pieces:
        steps = jax.random.uniform(jax.random.fold_in(jax.random.fold_in(rng, 6), axis_at), (blocks,), jnp.float32, least / len(pieces), top_value / len(pieces))
        factor_of = factor_of * jnp.repeat(jnp.exp(steps), shape[axis_at] // blocks).reshape((-1,) + (1,) * (len(shape) - 1 - axis_at))
    return factor_of


def deal_out(own_key, own, number, rows, count, top, most, slope):
    order = jax.random.permutation(own_key, count)
    packed, ordinary = portions_of(count, rows * top, most, slope, True), portions_of(count, rows * top, most, slope, False)
    places = jnp.arange(count)

    def named(tallies, turn):
        used = int((tallies > 0).sum())
        fixed = max(1, used // 4)
        shifted = fixed + (places - fixed + turn * (used - fixed)) % max(1, count - fixed)
        return jnp.zeros((count,), jnp.int32).at[order[jnp.where(places < fixed, places, shifted)]].set(jnp.asarray(tallies, jnp.int32))

    tallies = jnp.where(number % 4 == 0, named(packed, number // 4), named(ordinary, number - number // 4 - 1))
    mixed = jax.random.permutation(jax.random.fold_in(own, 3), count)
    giver, receiver = mixed[0:count // 2 * 2:2], mixed[1:count // 2 * 2:2]
    slack = jnp.minimum(tallies[giver] - 1, most - tallies[receiver]) // 2
    slack = jnp.where((giver == order[0]) | (receiver == order[0]) | (tallies[receiver] == 0), 0, jnp.maximum(slack, 0))
    shifted = jax.random.randint(jax.random.fold_in(own, 4), (count // 2,), 0, 1 << 20) % (slack + 1)
    tallies = tallies.at[giver].add(-shifted).at[receiver].add(shifted)
    items = jnp.searchsorted(jnp.cumsum(tallies), jnp.arange(rows * top), side="right").astype(jnp.int32)
    table = items.reshape(top, rows).T
    table = table[jax.random.permutation(jax.random.fold_in(own, 1), rows)]
    turn = jax.random.randint(jax.random.fold_in(own, 2), (rows, 1), 0, top)
    return jnp.take_along_axis(table, (jnp.arange(top)[None, :] + turn) % top, axis=1)


def portions_of(count, total, limit, lean, full):
    loads = [(1 << 20) // math.isqrt(rank ** lean) + 1 for rank in range(1, count + 1)]
    largest = limit if full else min(limit, max(-(-total // count), total * loads[0] // sum(loads)))
    least = 1 if total - largest >= count - 1 else 0
    given, spare = [largest] + [least] * (count - 1), total - largest - least * (count - 1)
    while spare > 0:
        free = [i for i in range(1, count) if given[i] < largest] or [i for i in range(1, count) if given[i] < limit]
        whole, budget = sum([loads[i] for i in free]), spare
        for i in free:
            extra = min(limit - given[i], max(1, budget * loads[i] // whole), spare)
            given[i] = given[i] + extra
            spare = spare - extra
    return np.array(given)


def bell_draw(own_key, extent, deviation, reach, cuts=(), held_as=jnp.bfloat16):
    drawn = jax.random.normal(own_key, extent, jnp.float32) * deviation
    if len(cuts) > 0:
        drawn = steps_of(own_key, extent, cuts, -0.22, 0.18) * drawn
    return jnp.clip(drawn, min=-reach, max=reach).astype(held_as)


def setup_inputs(seed: int = 0) -> dict:
    keys = jax.random.split(jax.random.key(seed), 11)
    embeddings = bell_draw(keys[0], (TOKENS, MODEL_WIDTH), 1.0, 6.0, ((0, 32),))
    norm_gain = jnp.clip(1.0 + 0.18 * jax.random.normal(keys[1], (MODEL_WIDTH,), jnp.float32), 0.099609375, 1.8984375).astype(jnp.bfloat16)
    query_key_value_weight = bell_draw(keys[2], (MODEL_WIDTH, KEY_VALUE_HEADS * (QUERY_HEADS // KEY_VALUE_HEADS + 2) * HEAD_SIZE), MODEL_WIDTH ** -0.5, 0.09375, ((1, 8),))
    embed_table = bell_draw(keys[3], (VOCAB, MODEL_WIDTH), 1.0, 6.0, ((0, 32), (1, 8)))
    rotated_cache_pages = draw_rotated_cache_pages(jax.random.fold_in(keys[10], 71), 0)
    page_owner_device = jax.vmap(lambda own: jax.random.permutation(own, REQUEST_COUNT))(jax.random.split(keys[5], REQUEST_COUNT)).reshape((REQUEST_COUNT, REQUEST_COUNT)).astype(jnp.int32)
    cached_length = draw_cached_length(jax.random.fold_in(keys[10], 71), 0)
    vocab_shard_keys = jax.random.split(jax.random.fold_in(keys[7], 1), TOKENS // BLOCK_TOKENS)
    vocab_shard_turns = jax.random.permutation(jax.random.fold_in(keys[7], 3), TOKENS // BLOCK_TOKENS)
    vocab_shard = jax.vmap(lambda own, number: deal_out(jax.random.fold_in(keys[7], 2), own, number, BLOCK_TOKENS, REQUEST_COUNT, 1, CAP, 1))(vocab_shard_keys, vocab_shard_turns).reshape((TOKENS, 1))
    shard_row = with_ends(jax.random.randint(keys[8], (TOKENS,), 0, SHARD_ROWS), jax.random.fold_in(keys[8], 1), 0, SHARD_ROWS - 1).astype(jnp.int32)
    accept = draw_accept(jax.random.fold_in(keys[10], 71), 0)
    return dict(embeddings=embeddings, norm_gain=norm_gain, query_key_value_weight=query_key_value_weight, embed_table=embed_table, rotated_cache_pages=rotated_cache_pages, page_owner_device=page_owner_device, cached_length=cached_length, vocab_shard=vocab_shard, shard_row=shard_row, accept=accept)


THETA = 500000.0

def angles(positions):
    steps_half = jnp.arange(HEAD_SIZE // 2, dtype=jnp.float32)
    frequency = THETA ** (-(steps_half * 2.0) / HEAD_SIZE)
    return positions.astype(jnp.float32)[:, None] * frequency[None, :]

def rotate(vectors, turning):
    half_width = vectors.shape[-1] // 2
    former = vectors[..., :half_width]
    latter = vectors[..., half_width:]
    cosine = jnp.cos(turning)
    sine_of = jnp.sin(turning)
    return jnp.concatenate([former * cosine - latter * sine_of, latter * cosine + former * sine_of], axis=-1)

def project(inputs, norm_gain, query_key_value_weight, positions):
    widened = inputs.astype(jnp.float32)
    inverse = lax.rsqrt(lax.optimization_barrier(jnp.mean(widened * widened, axis=-1, keepdims=True)) + 1e-05)
    normed = (widened * inverse * norm_gain.astype(jnp.float32)).astype(jnp.bfloat16)
    combined = jnp.dot(normed, query_key_value_weight, preferred_element_type=jnp.float32)
    heads_per_group = QUERY_HEADS // KEY_VALUE_HEADS
    combined = combined.reshape(inputs.shape[0], -1, heads_per_group + 2, HEAD_SIZE)
    turning = angles(positions)[:, None, None, :]
    query_vectors = rotate(combined[:, :, :heads_per_group], turning).astype(jnp.bfloat16)
    block_keys = rotate(combined[:, :, heads_per_group:heads_per_group + 1], turning)[:, :, 0].astype(jnp.bfloat16)
    block_values = combined[:, :, heads_per_group + 1].astype(jnp.bfloat16)
    return (query_vectors, block_keys, block_values)

def attend(query_vectors, block_keys, block_values, page_keys, page_values, usable):
    factor = 1.0 / math.sqrt(HEAD_SIZE)
    query_wide = query_vectors.astype(jnp.float32)
    scores_cache = jnp.einsum('bgqd,kgd->gqbk', query_wide, page_keys.astype(jnp.float32)) * factor
    scores_cache = jnp.where(usable[None, None, None, :], scores_cache, -1e+30)
    scores_block = jnp.einsum('bgqd,cgd->gqbc', query_wide, block_keys.astype(jnp.float32)) * factor
    highest = jnp.maximum(lax.optimization_barrier(jnp.max(scores_cache, axis=-1)), lax.optimization_barrier(jnp.max(scores_block, axis=-1)))[..., None]
    exp_cache = jnp.exp(scores_cache - highest)
    exp_block = jnp.exp(scores_block - highest)
    totals = lax.optimization_barrier(jnp.sum(exp_cache, axis=-1)) + lax.optimization_barrier(jnp.sum(exp_block, axis=-1))
    weights_cache = lax.optimization_barrier(exp_cache.astype(jnp.bfloat16)).astype(jnp.float32)
    weights_block = lax.optimization_barrier(exp_block.astype(jnp.bfloat16)).astype(jnp.float32)
    combined = jnp.einsum('gqbk,kgd->bgqd', weights_cache, page_values.astype(jnp.float32))
    combined = combined + jnp.einsum('gqbc,cgd->bgqd', weights_block, block_values.astype(jnp.float32))
    result = combined / jnp.transpose(totals, (2, 0, 1))[..., None]
    return result.astype(jnp.bfloat16).reshape(query_vectors.shape[0], -1)

def reference(embeddings, norm_gain, query_key_value_weight, embed_table, rotated_cache_pages, page_owner_device, cached_length, vocab_shard, shard_row, accept):
    offsets = jnp.arange(BLOCK_TOKENS, dtype=jnp.int32)
    positions = (cached_length[:, None] + offsets[None, :]).reshape(-1)
    chosen_ids = (vocab_shard[:, 0] * SHARD_ROWS + shard_row).astype(jnp.int32)
    replaced = jnp.where(accept[:, None] == 1, jnp.take(embed_table, chosen_ids, axis=0), embeddings)
    page_spots = jnp.arange(PAGE_POSITIONS, dtype=jnp.int32)
    key_spots = (jnp.arange(REQUEST_COUNT, dtype=jnp.int32)[:, None] * PAGE_POSITIONS + page_spots[None, :]).reshape(-1)
    heads_per_group = QUERY_HEADS // KEY_VALUE_HEADS
    results = []
    for inputs in (embeddings, replaced):
        query_vectors, block_keys, block_values = project(inputs, norm_gain, query_key_value_weight, positions)

        def request(packed_pages):
            query_rows, key_rows, value_rows, holder_devices, length, request_number = packed_pages
            page_row_entries = rotated_cache_pages[holder_devices, request_number].reshape(REQUEST_COUNT * PAGE_POSITIONS, KEY_VALUE_HEADS, 2, HEAD_SIZE)
            return attend(query_rows, key_rows, value_rows, page_row_entries[:, :, 0], page_row_entries[:, :, 1], key_spots < length)
        packed_pages = (query_vectors.reshape(REQUEST_COUNT, BLOCK_TOKENS, KEY_VALUE_HEADS, heads_per_group, HEAD_SIZE), block_keys.reshape(REQUEST_COUNT, BLOCK_TOKENS, KEY_VALUE_HEADS, HEAD_SIZE), block_values.reshape(REQUEST_COUNT, BLOCK_TOKENS, KEY_VALUE_HEADS, HEAD_SIZE), page_owner_device, cached_length, jnp.arange(REQUEST_COUNT, dtype=jnp.int32))
        results.append(lax.map(request, packed_pages).reshape(TOKENS, QUERY_HEADS * HEAD_SIZE))
    return (results[0], results[1])
```

```python
import math

import jax
import jax.numpy as jnp
from jax import lax
from jax.experimental import pallas as pl
from jax.experimental.pallas import tpu as pltpu
from jax.sharding import PartitionSpec as P

QUERY_HEADS = 32
KEY_VALUE_HEADS = 8
HEAD_SIZE = 128
HEADS_PER_GROUP = QUERY_HEADS // KEY_VALUE_HEADS


THETA = 500000.0
KEY_CHUNK = 1024


def angles(positions):
    steps_half = jnp.arange(HEAD_SIZE // 2, dtype=jnp.float32)
    frequency = THETA ** (-(steps_half * 2.0) / HEAD_SIZE)
    return positions.astype(jnp.float32)[:, None] * frequency[None, :]


def rotate(vectors, turning):
    half_width = vectors.shape[-1] // 2
    former = vectors[..., :half_width]
    latter = vectors[..., half_width:]
    cosine = jnp.cos(turning)
    sine_of = jnp.sin(turning)
    return jnp.concatenate(
        [former * cosine - latter * sine_of, latter * cosine + former * sine_of], axis=-1
    )


def project(inputs, norm_gain, query_key_value_weight, positions):
    widened = inputs.astype(jnp.float32)
    inverse = lax.rsqrt(jnp.mean(widened * widened, axis=-1, keepdims=True) + 1e-05)
    normed = (widened * inverse * norm_gain.astype(jnp.float32)).astype(jnp.bfloat16)
    combined = jnp.dot(normed, query_key_value_weight, preferred_element_type=jnp.float32)
    rows = inputs.shape[0]
    combined = combined.reshape(rows, -1, HEADS_PER_GROUP + 2, HEAD_SIZE)
    turning = angles(positions)[:, None, None, :]
    query_vectors = rotate(combined[:, :, :HEADS_PER_GROUP], turning).astype(jnp.bfloat16)
    block_keys = rotate(combined[:, :, HEADS_PER_GROUP : HEADS_PER_GROUP + 1], turning)[
        :, :, 0
    ].astype(jnp.bfloat16)
    block_values = combined[:, :, HEADS_PER_GROUP + 1].astype(jnp.bfloat16)
    return (
        query_vectors.reshape(rows, -1),
        block_keys.reshape(rows, -1),
        block_values.reshape(rows, -1),
    )


def attention_kernel(q1_ref, q2_ref, kb1_ref, vb1_ref, kb2_ref, vb2_ref, pg_ref, us_ref,
                     o1_ref, o2_ref, s_ref):
    factor = 1.0 / math.sqrt(HEAD_SIZE)
    nt = (((1,), (1,)), ((), ()))
    rows = q1_ref.shape[0]
    q = jnp.concatenate([q1_ref[...], q2_ref[...]], axis=0)
    sb1 = lax.dot_general(q1_ref[...], kb1_ref[...], nt, preferred_element_type=jnp.float32) * factor
    sb2 = lax.dot_general(q2_ref[...], kb2_ref[...], nt, preferred_element_type=jnp.float32) * factor
    high = jnp.concatenate(
        [jnp.max(sb1, axis=1, keepdims=True), jnp.max(sb2, axis=1, keepdims=True)], axis=0
    )
    keys_total = pg_ref.shape[0]
    chunks = keys_total // KEY_CHUNK
    for c in range(chunks):
        lo = c * KEY_CHUNK
        k = pg_ref[lo : lo + KEY_CHUNK, 0:HEAD_SIZE]
        sc = lax.dot_general(q, k, nt, preferred_element_type=jnp.float32) * factor
        sc = jnp.where(us_ref[:, lo : lo + KEY_CHUNK] > 0, sc, -1e30)
        s_ref[:, lo : lo + KEY_CHUNK] = sc
        high = jnp.maximum(high, jnp.max(sc, axis=1, keepdims=True))
    h1 = high[:rows]
    h2 = high[rows:]
    eb1 = jnp.exp(sb1 - h1)
    eb2 = jnp.exp(sb2 - h2)
    tot = jnp.concatenate(
        [jnp.sum(eb1, axis=1, keepdims=True), jnp.sum(eb2, axis=1, keepdims=True)], axis=0
    )
    acc = jnp.concatenate(
        [
            jnp.dot(eb1.astype(jnp.bfloat16), vb1_ref[...], preferred_element_type=jnp.float32),
            jnp.dot(eb2.astype(jnp.bfloat16), vb2_ref[...], preferred_element_type=jnp.float32),
        ],
        axis=0,
    )
    for c in range(chunks):
        lo = c * KEY_CHUNK
        e = jnp.exp(s_ref[:, lo : lo + KEY_CHUNK] - high)
        tot = tot + jnp.sum(e, axis=1, keepdims=True)
        v = pg_ref[lo : lo + KEY_CHUNK, HEAD_SIZE : 2 * HEAD_SIZE]
        acc = acc + jnp.dot(e.astype(jnp.bfloat16), v, preferred_element_type=jnp.float32)
    res = (acc / tot).astype(jnp.bfloat16)
    o1_ref[...] = res[:rows]
    o2_ref[...] = res[rows:]


def attend_both(q1, kb1, vb1, q2, kb2, vb2, pages, usable):
    rows = q1.shape[0]
    keys_total = pages.shape[0]
    qspec = pl.BlockSpec((rows, HEAD_SIZE), lambda j: (0, j))
    full = pl.BlockSpec((rows, HEAD_SIZE), lambda j: (0, 0))
    return pl.pallas_call(
        attention_kernel,
        grid=(HEADS_PER_GROUP,),
        in_specs=[
            qspec,
            qspec,
            full,
            full,
            full,
            full,
            pl.BlockSpec((keys_total, 2 * HEAD_SIZE), lambda j: (0, 0)),
            pl.BlockSpec((1, keys_total), lambda j: (0, 0)),
        ],
        out_specs=[qspec, qspec],
        out_shape=[
            jax.ShapeDtypeStruct(q1.shape, jnp.bfloat16),
            jax.ShapeDtypeStruct(q1.shape, jnp.bfloat16),
        ],
        scratch_shapes=[pltpu.VMEM((2 * rows, keys_total), jnp.float32)],
        compiler_params=pltpu.CompilerParams(vmem_limit_bytes=48 * 1024 * 1024),
    )(q1, q2, kb1, vb1, kb2, vb2, pages, usable)


def body(
    embeddings,
    norm_gain,
    query_key_value_weight,
    embed_table,
    rotated_cache_pages,
    page_owner_device,
    cached_length,
    vocab_shard,
    shard_row,
    accept,
):
    members = lax.axis_size("tok")
    length = embeddings.shape[0]
    sources = jnp.arange(members, dtype=jnp.int32)
    positions = cached_length[0] + jnp.arange(length, dtype=jnp.int32)
    arrived = lax.all_to_all(rotated_cache_pages, "tok", split_axis=1, concat_axis=0, tiled=True)
    page_size = arrived.shape[2]
    pages = arrived.reshape(members * page_size, -1)
    page_index = jnp.sum(
        jnp.where(page_owner_device[0][:, None] == sources[None, :], sources[:, None], 0), axis=0
    )
    page_spots = page_index[:, None] * page_size + jnp.arange(page_size, dtype=jnp.int32)[None, :]
    usable = (page_spots.reshape(1, -1) < cached_length[0]).astype(jnp.float32)

    query_vectors, block_keys, block_values = project(
        embeddings, norm_gain, query_key_value_weight, positions
    )
    target_shard = vocab_shard[:, 0]
    capacity = max(2, 2 * length // members)
    chosen = (target_shard[:, None] == sources[None, :]).astype(jnp.int32)
    earlier = (jnp.arange(length)[:, None] > jnp.arange(length)[None, :]).astype(jnp.int32)
    slot_rank = jnp.sum(jnp.dot(earlier, chosen) * chosen, axis=1)
    wanted = jnp.zeros((members, capacity), jnp.int32).at[target_shard, slot_rank].set(shard_row)
    asked = lax.all_to_all(wanted, "tok", split_axis=0, concat_axis=0, tiled=True)
    found_rows = jnp.take(embed_table, asked, axis=0)
    returned = lax.all_to_all(found_rows, "tok", split_axis=0, concat_axis=0, tiled=True)
    replacement = returned[target_shard, slot_rank]
    full_rows = lax.all_gather(replacement, "head", axis=1, tiled=True)
    replaced = jnp.where(accept[:, None] == 1, full_rows, embeddings)
    queries_two, keys_two, values_two = project(
        replaced, norm_gain, query_key_value_weight, positions
    )
    return attend_both(
        query_vectors, block_keys, block_values, queries_two, keys_two, values_two, pages, usable
    )


def solution(mesh):
    return jax.shard_map(
        body,
        mesh=mesh,
        in_specs=(
            P("tok", None),
            P(),
            P(None, "head"),
            P("tok", "head"),
            P("tok", None, None, "head"),
            P("tok", None),
            P("tok"),
            P("tok", None),
            P("tok"),
            P("tok"),
        ),
        out_specs=(P("tok", "head"), P("tok", "head")),
        check_vma=False,
    )
```

```python
import math

import jax
import jax.numpy as jnp
from jax import lax
from jax.experimental import pallas as pl
from jax.experimental.pallas import tpu as pltpu
from jax.sharding import PartitionSpec as P


QUERY_HEADS = 32
KEY_VALUE_HEADS = 8
HEAD_SIZE = 128
HEADS_PER_GROUP = QUERY_HEADS // KEY_VALUE_HEADS


THETA = 500000.0


def angles(positions):
    steps_half = jnp.arange(HEAD_SIZE // 2, dtype=jnp.float32)
    frequency = THETA ** (-(steps_half * 2.0) / HEAD_SIZE)
    return positions.astype(jnp.float32)[:, None] * frequency[None, :]


def rotate(vectors, turning):
    half_width = vectors.shape[-1] // 2
    former = vectors[..., :half_width]
    latter = vectors[..., half_width:]
    cosine = jnp.cos(turning)
    sine_of = jnp.sin(turning)
    return jnp.concatenate(
        [former * cosine - latter * sine_of, latter * cosine + former * sine_of], axis=-1
    )


def project(inputs, norm_gain, query_key_value_weight, positions):
    widened = inputs.astype(jnp.float32)
    inverse = lax.rsqrt(jnp.mean(widened * widened, axis=-1, keepdims=True) + 1e-05)
    normed = (widened * inverse * norm_gain.astype(jnp.float32)).astype(jnp.bfloat16)
    combined = jnp.dot(normed, query_key_value_weight, preferred_element_type=jnp.float32)
    rows = inputs.shape[0]
    combined = combined.reshape(rows, -1, HEADS_PER_GROUP + 2, HEAD_SIZE)
    turning = angles(positions)[:, None, None, :]
    query_vectors = rotate(combined[:, :, :HEADS_PER_GROUP], turning).astype(jnp.bfloat16)
    block_keys = rotate(combined[:, :, HEADS_PER_GROUP : HEADS_PER_GROUP + 1], turning)[
        :, :, 0
    ].astype(jnp.bfloat16)
    block_values = combined[:, :, HEADS_PER_GROUP + 1].astype(jnp.bfloat16)
    return (
        query_vectors.reshape(rows, -1),
        block_keys.reshape(rows, -1),
        block_values.reshape(rows, -1),
    )


def attention_kernel(q1_ref, q2_ref, kb1_ref, vb1_ref, kb2_ref, vb2_ref, us_ref, *rest):
    o1_ref, o2_ref, s_ref = rest[-3:]
    page_refs = rest[:-3]
    factor = 1.0 / math.sqrt(HEAD_SIZE)
    nt = (((1,), (1,)), ((), ()))
    rows = q1_ref.shape[0]
    q = jnp.concatenate([q1_ref[...], q2_ref[...]], axis=0)
    sb1 = lax.dot_general(q1_ref[...], kb1_ref[...], nt, preferred_element_type=jnp.float32) * factor
    sb2 = lax.dot_general(q2_ref[...], kb2_ref[...], nt, preferred_element_type=jnp.float32) * factor
    high = jnp.concatenate(
        [jnp.max(sb1, axis=1, keepdims=True), jnp.max(sb2, axis=1, keepdims=True)], axis=0
    )
    chunk = page_refs[0].shape[0]
    for c, pg_ref in enumerate(page_refs):
        lo = c * chunk
        k = pg_ref[:, 0:HEAD_SIZE]
        sc = lax.dot_general(q, k, nt, preferred_element_type=jnp.float32) * factor
        sc = jnp.where(us_ref[:, lo : lo + chunk] > 0, sc, -1e30)
        s_ref[:, lo : lo + chunk] = sc
        high = jnp.maximum(high, jnp.max(sc, axis=1, keepdims=True))
    h1 = high[:rows]
    h2 = high[rows:]
    eb1 = jnp.exp(sb1 - h1)
    eb2 = jnp.exp(sb2 - h2)
    tot = jnp.concatenate(
        [jnp.sum(eb1, axis=1, keepdims=True), jnp.sum(eb2, axis=1, keepdims=True)], axis=0
    )
    acc = jnp.concatenate(
        [
            jnp.dot(eb1.astype(jnp.bfloat16), vb1_ref[...], preferred_element_type=jnp.float32),
            jnp.dot(eb2.astype(jnp.bfloat16), vb2_ref[...], preferred_element_type=jnp.float32),
        ],
        axis=0,
    )
    for c, pg_ref in enumerate(page_refs):
        lo = c * chunk
        e = jnp.exp(s_ref[:, lo : lo + chunk] - high)
        tot = tot + jnp.sum(e, axis=1, keepdims=True)
        v = pg_ref[:, HEAD_SIZE : 2 * HEAD_SIZE]
        acc = acc + jnp.dot(e.astype(jnp.bfloat16), v, preferred_element_type=jnp.float32)
    res = (acc / tot).astype(jnp.bfloat16)
    o1_ref[...] = res[:rows]
    o2_ref[...] = res[rows:]


def attend_both(q1, kb1, vb1, q2, kb2, vb2, pages, usable):
    rows = q1.shape[0]
    page_size = pages[0].shape[0]
    keys_total = page_size * len(pages)
    qspec = pl.BlockSpec((rows, HEAD_SIZE), lambda j: (0, j))
    full = pl.BlockSpec((rows, HEAD_SIZE), lambda j: (0, 0))
    return pl.pallas_call(
        attention_kernel,
        grid=(HEADS_PER_GROUP,),
        in_specs=[
            qspec,
            qspec,
            full,
            full,
            full,
            full,
            pl.BlockSpec((1, keys_total), lambda j: (0, 0)),
        ]
        + [pl.BlockSpec((page_size, 2 * HEAD_SIZE), lambda j: (0, 0)) for _ in pages],
        out_specs=[qspec, qspec],
        out_shape=[
            jax.ShapeDtypeStruct(q1.shape, jnp.bfloat16),
            jax.ShapeDtypeStruct(q1.shape, jnp.bfloat16),
        ],
        scratch_shapes=[pltpu.VMEM((2 * rows, keys_total), jnp.float32)],
        compiler_params=pltpu.CompilerParams(vmem_limit_bytes=48 * 1024 * 1024),
    )(q1, q2, kb1, vb1, kb2, vb2, usable, *pages)


def body(
    embeddings,
    norm_gain,
    query_key_value_weight,
    embed_table,
    rotated_cache_pages,
    page_owner_device,
    cached_length,
    vocab_shard,
    shard_row,
    accept,
):
    members = lax.axis_size("tok")
    length = embeddings.shape[0]
    sources = jnp.arange(members, dtype=jnp.int32)
    positions = cached_length[0] + jnp.arange(length, dtype=jnp.int32)
    me = lax.axis_index("tok")
    held = rotated_cache_pages[0]
    page_size = held.shape[1]
    pages = [lax.dynamic_index_in_dim(held, me, 0, keepdims=False)]
    for shift in range(1, members):
        outgoing = lax.dynamic_index_in_dim(held, (me + shift) % members, 0, keepdims=False)
        pages.append(
            lax.ppermute(
                outgoing, "tok", [(i, (i + shift) % members) for i in range(members)]
            )
        )
    page_index = jnp.sum(
        jnp.where(page_owner_device[0][:, None] == sources[None, :], sources[:, None], 0), axis=0
    )
    source_of = (me - sources) % members
    page_index = page_index[source_of]
    page_spots = page_index[:, None] * page_size + jnp.arange(page_size, dtype=jnp.int32)[None, :]
    usable = (page_spots.reshape(1, -1) < cached_length[0]).astype(jnp.float32)

    query_vectors, block_keys, block_values = project(
        embeddings, norm_gain, query_key_value_weight, positions
    )
    target_shard = vocab_shard[:, 0]
    capacity = max(2, 2 * length // members)
    chosen = (target_shard[:, None] == sources[None, :]).astype(jnp.int32)
    earlier = (jnp.arange(length)[:, None] > jnp.arange(length)[None, :]).astype(jnp.int32)
    slot_rank = jnp.sum(jnp.dot(earlier, chosen) * chosen, axis=1)
    wanted = jnp.zeros((members, capacity), jnp.int32).at[target_shard, slot_rank].set(shard_row)
    asked = lax.all_to_all(wanted, "tok", split_axis=0, concat_axis=0, tiled=True)
    found_rows = jnp.take(embed_table, asked, axis=0)
    returned = lax.all_to_all(found_rows, "tok", split_axis=0, concat_axis=0, tiled=True)
    replacement = returned[target_shard, slot_rank]
    full_rows = lax.all_gather(replacement, "head", axis=1, tiled=True)
    replaced = jnp.where(accept[:, None] == 1, full_rows, embeddings)
    queries_two, keys_two, values_two = project(
        replaced, norm_gain, query_key_value_weight, positions
    )
    return attend_both(
        query_vectors, block_keys, block_values, queries_two, keys_two, values_two, pages, usable
    )


def solution(mesh):
    return jax.shard_map(
        body,
        mesh=mesh,
        in_specs=(
            P("tok", None),
            P(),
            P(None, "head"),
            P("tok", "head"),
            P("tok", None, None, "head"),
            P("tok", None),
            P("tok"),
            P("tok", None),
            P("tok"),
            P("tok"),
        ),
        out_specs=(P("tok", "head"), P("tok", "head")),
        check_vma=False,
    )
```

```python
import math

import jax
import jax.numpy as jnp
from jax import lax
from jax.experimental import pallas as pl
from jax.experimental.pallas import tpu as pltpu
from jax.sharding import PartitionSpec as P


QUERY_HEADS = 32
KEY_VALUE_HEADS = 8
HEAD_SIZE = 128
HEADS_PER_GROUP = QUERY_HEADS // KEY_VALUE_HEADS


THETA = 500000.0
KEY_CHUNK = 1024


def angles(positions):
    steps_half = jnp.arange(HEAD_SIZE // 2, dtype=jnp.float32)
    frequency = THETA ** (-(steps_half * 2.0) / HEAD_SIZE)
    return positions.astype(jnp.float32)[:, None] * frequency[None, :]


def rotate(vectors, turning):
    half_width = vectors.shape[-1] // 2
    former = vectors[..., :half_width]
    latter = vectors[..., half_width:]
    cosine = jnp.cos(turning)
    sine_of = jnp.sin(turning)
    return jnp.concatenate(
        [former * cosine - latter * sine_of, latter * cosine + former * sine_of], axis=-1
    )


def project(inputs, norm_gain, query_key_value_weight, positions):
    widened = inputs.astype(jnp.float32)
    inverse = lax.rsqrt(jnp.mean(widened * widened, axis=-1, keepdims=True) + 1e-05)
    normed = (widened * inverse * norm_gain.astype(jnp.float32)).astype(jnp.bfloat16)
    combined = jnp.dot(normed, query_key_value_weight, preferred_element_type=jnp.float32)
    rows = inputs.shape[0]
    combined = combined.reshape(rows, -1, HEADS_PER_GROUP + 2, HEAD_SIZE)
    turning = angles(positions)[:, None, None, :]
    query_vectors = rotate(combined[:, :, :HEADS_PER_GROUP], turning).astype(jnp.bfloat16)
    block_keys = rotate(combined[:, :, HEADS_PER_GROUP : HEADS_PER_GROUP + 1], turning)[
        :, :, 0
    ].astype(jnp.bfloat16)
    block_values = combined[:, :, HEADS_PER_GROUP + 1].astype(jnp.bfloat16)
    return (
        query_vectors.reshape(rows, -1),
        block_keys.reshape(rows, -1),
        block_values.reshape(rows, -1),
    )


def attention_kernel(q1_ref, q2_ref, kb1_ref, vb1_ref, kb2_ref, vb2_ref, pg_ref, us_ref,
                     o1_ref, o2_ref, s_ref):
    factor = 1.0 / math.sqrt(HEAD_SIZE)
    nt = (((1,), (1,)), ((), ()))
    rows = q1_ref.shape[0]
    q = jnp.concatenate([q1_ref[...], q2_ref[...]], axis=0)
    sb1 = lax.dot_general(q1_ref[...], kb1_ref[...], nt, preferred_element_type=jnp.float32) * factor
    sb2 = lax.dot_general(q2_ref[...], kb2_ref[...], nt, preferred_element_type=jnp.float32) * factor
    high = jnp.concatenate(
        [jnp.max(sb1, axis=1, keepdims=True), jnp.max(sb2, axis=1, keepdims=True)], axis=0
    )
    keys_total = pg_ref.shape[0]
    chunks = keys_total // KEY_CHUNK
    for c in range(chunks):
        lo = c * KEY_CHUNK
        k = pg_ref[lo : lo + KEY_CHUNK, 0:HEAD_SIZE]
        sc = lax.dot_general(q, k, nt, preferred_element_type=jnp.float32) * factor
        sc = jnp.where(us_ref[:, lo : lo + KEY_CHUNK] > 0, sc, -1e30)
        s_ref[:, lo : lo + KEY_CHUNK] = sc
        high = jnp.maximum(high, jnp.max(sc, axis=1, keepdims=True))
    h1 = high[:rows]
    h2 = high[rows:]
    eb1 = jnp.exp(sb1 - h1)
    eb2 = jnp.exp(sb2 - h2)
    tot = jnp.concatenate(
        [jnp.sum(eb1, axis=1, keepdims=True), jnp.sum(eb2, axis=1, keepdims=True)], axis=0
    )
    acc = jnp.concatenate(
        [
            jnp.dot(eb1.astype(jnp.bfloat16), vb1_ref[...], preferred_element_type=jnp.float32),
            jnp.dot(eb2.astype(jnp.bfloat16), vb2_ref[...], preferred_element_type=jnp.float32),
        ],
        axis=0,
    )
    for c in range(chunks):
        lo = c * KEY_CHUNK
        e = jnp.exp(s_ref[:, lo : lo + KEY_CHUNK] - high)
        tot = tot + jnp.sum(e, axis=1, keepdims=True)
        v = pg_ref[lo : lo + KEY_CHUNK, HEAD_SIZE : 2 * HEAD_SIZE]
        acc = acc + jnp.dot(e.astype(jnp.bfloat16), v, preferred_element_type=jnp.float32)
    res = (acc / tot).astype(jnp.bfloat16)
    o1_ref[...] = res[:rows]
    o2_ref[...] = res[rows:]


def attend_both(q1, kb1, vb1, q2, kb2, vb2, pages, usable):
    rows = q1.shape[0]
    keys_total = pages.shape[0]
    qspec = pl.BlockSpec((rows, HEAD_SIZE), lambda j: (0, j))
    full = pl.BlockSpec((rows, HEAD_SIZE), lambda j: (0, 0))
    return pl.pallas_call(
        attention_kernel,
        grid=(HEADS_PER_GROUP,),
        in_specs=[
            qspec,
            qspec,
            full,
            full,
            full,
            full,
            pl.BlockSpec((keys_total, 2 * HEAD_SIZE), lambda j: (0, 0)),
            pl.BlockSpec((1, keys_total), lambda j: (0, 0)),
        ],
        out_specs=[qspec, qspec],
        out_shape=[
            jax.ShapeDtypeStruct(q1.shape, jnp.bfloat16),
            jax.ShapeDtypeStruct(q1.shape, jnp.bfloat16),
        ],
        scratch_shapes=[pltpu.VMEM((2 * rows, keys_total), jnp.float32)],
        compiler_params=pltpu.CompilerParams(vmem_limit_bytes=48 * 1024 * 1024),
    )(q1, q2, kb1, vb1, kb2, vb2, pages, usable)


def body(
    embeddings,
    norm_gain,
    query_key_value_weight,
    embed_table,
    rotated_cache_pages,
    page_owner_device,
    cached_length,
    vocab_shard,
    shard_row,
    accept,
):
    members = lax.axis_size("tok")
    length = embeddings.shape[0]
    sources = jnp.arange(members, dtype=jnp.int32)
    positions = cached_length[0] + jnp.arange(length, dtype=jnp.int32)
    arrived = lax.all_to_all(rotated_cache_pages, "tok", split_axis=1, concat_axis=0, tiled=True)
    page_size = arrived.shape[2]
    pages = arrived.reshape(members * page_size, -1)
    page_index = jnp.sum(
        jnp.where(page_owner_device[0][:, None] == sources[None, :], sources[:, None], 0), axis=0
    )
    page_spots = page_index[:, None] * page_size + jnp.arange(page_size, dtype=jnp.int32)[None, :]
    usable = (page_spots.reshape(1, -1) < cached_length[0]).astype(jnp.float32)

    query_vectors, block_keys, block_values = project(
        embeddings, norm_gain, query_key_value_weight, positions
    )
    target_shard = vocab_shard[:, 0]
    capacity = max(2, 2 * length // members)
    me = lax.axis_index("tok")
    chosen = (target_shard[:, None] == sources[None, :]).astype(jnp.int32)
    earlier = (jnp.arange(length)[:, None] > jnp.arange(length)[None, :]).astype(jnp.int32)
    slot_rank = jnp.sum(jnp.dot(earlier, chosen) * chosen, axis=1)
    slot_of = target_shard * capacity + slot_rank
    slots = jnp.arange(members * capacity, dtype=jnp.int32)
    wanted = jnp.sum(
        jnp.where(slot_of[:, None] == slots[None, :], shard_row[:, None], 0), axis=0
    ).reshape(members, capacity)
    every_wanted = lax.all_gather(wanted, "tok", axis=0, tiled=False)
    asked = every_wanted[:, me]
    found_rows = jnp.take(embed_table, asked, axis=0)
    arrived_rows = [lax.dynamic_index_in_dim(found_rows, me, 0, keepdims=False)]
    for shift in range(1, members):
        outgoing = lax.dynamic_index_in_dim(found_rows, (me + shift) % members, 0, keepdims=False)
        arrived_rows.append(
            lax.ppermute(
                outgoing, "tok", [(i, (i + shift) % members) for i in range(members)]
            )
        )
    returned = jnp.stack(arrived_rows, axis=0)
    replacement = returned[(me - target_shard) % members, slot_rank]
    full_rows = lax.all_gather(replacement, "head", axis=1, tiled=True)
    replaced = jnp.where(accept[:, None] == 1, full_rows, embeddings)
    queries_two, keys_two, values_two = project(
        replaced, norm_gain, query_key_value_weight, positions
    )
    return attend_both(
        query_vectors, block_keys, block_values, queries_two, keys_two, values_two, pages, usable
    )


def solution(mesh):
    return jax.shard_map(
        body,
        mesh=mesh,
        in_specs=(
            P("tok", None),
            P(),
            P(None, "head"),
            P("tok", "head"),
            P("tok", None, None, "head"),
            P("tok", None),
            P("tok"),
            P("tok", None),
            P("tok"),
            P("tok"),
        ),
        out_specs=(P("tok", "head"), P("tok", "head")),
        check_vma=False,
    )
```

```python
import math

import jax
import jax.numpy as jnp
from jax import lax
from jax.experimental import pallas as pl
from jax.experimental.pallas import tpu as pltpu
from jax.sharding import PartitionSpec as P

QUERY_HEADS = 32
KEY_VALUE_HEADS = 8
HEAD_SIZE = 128
HEADS_PER_GROUP = QUERY_HEADS // KEY_VALUE_HEADS


THETA = 500000.0
KEY_CHUNK = 1024


def angles(positions):
    steps_half = jnp.arange(HEAD_SIZE // 2, dtype=jnp.float32)
    frequency = THETA ** (-(steps_half * 2.0) / HEAD_SIZE)
    return positions.astype(jnp.float32)[:, None] * frequency[None, :]


def rotate(vectors, turning):
    half_width = vectors.shape[-1] // 2
    former = vectors[..., :half_width]
    latter = vectors[..., half_width:]
    cosine = jnp.cos(turning)
    sine_of = jnp.sin(turning)
    return jnp.concatenate(
        [former * cosine - latter * sine_of, latter * cosine + former * sine_of], axis=-1
    )


def project(inputs, norm_gain, query_key_value_weight, positions):
    widened = inputs.astype(jnp.float32)
    inverse = lax.rsqrt(jnp.mean(widened * widened, axis=-1, keepdims=True) + 1e-05)
    normed = (widened * inverse * norm_gain.astype(jnp.float32)).astype(jnp.bfloat16)
    combined = jnp.dot(normed, query_key_value_weight, preferred_element_type=jnp.float32)
    rows = inputs.shape[0]
    combined = combined.reshape(rows, -1, HEADS_PER_GROUP + 2, HEAD_SIZE)
    turning = angles(positions)[:, None, None, :]
    query_vectors = rotate(combined[:, :, :HEADS_PER_GROUP], turning).astype(jnp.bfloat16)
    block_keys = rotate(combined[:, :, HEADS_PER_GROUP : HEADS_PER_GROUP + 1], turning)[
        :, :, 0
    ].astype(jnp.bfloat16)
    block_values = combined[:, :, HEADS_PER_GROUP + 1].astype(jnp.bfloat16)
    return (
        query_vectors.reshape(rows, -1),
        block_keys.reshape(rows, -1),
        block_values.reshape(rows, -1),
    )


def attention_kernel(q1_ref, q2_ref, kb1_ref, vb1_ref, kb2_ref, vb2_ref, pg_ref, us_ref,
                     o1_ref, o2_ref, s_ref):
    factor = 1.0 / math.sqrt(HEAD_SIZE)
    nt = (((1,), (1,)), ((), ()))
    rows = q1_ref.shape[0]
    q = jnp.concatenate([q1_ref[...], q2_ref[...]], axis=0)
    sb1 = lax.dot_general(q1_ref[...], kb1_ref[...], nt, preferred_element_type=jnp.float32) * factor
    sb2 = lax.dot_general(q2_ref[...], kb2_ref[...], nt, preferred_element_type=jnp.float32) * factor
    high = jnp.concatenate(
        [jnp.max(sb1, axis=1, keepdims=True), jnp.max(sb2, axis=1, keepdims=True)], axis=0
    )
    keys_total = pg_ref.shape[0]
    chunks = keys_total // KEY_CHUNK
    for c in range(chunks):
        lo = c * KEY_CHUNK
        k = pg_ref[lo : lo + KEY_CHUNK, 0:HEAD_SIZE]
        sc = lax.dot_general(q, k, nt, preferred_element_type=jnp.float32) * factor
        sc = jnp.where(us_ref[:, lo : lo + KEY_CHUNK] > 0, sc, -1e30)
        s_ref[:, lo : lo + KEY_CHUNK] = sc
        high = jnp.maximum(high, jnp.max(sc, axis=1, keepdims=True))
    h1 = high[:rows]
    h2 = high[rows:]
    eb1 = jnp.exp(sb1 - h1)
    eb2 = jnp.exp(sb2 - h2)
    tot = jnp.concatenate(
        [jnp.sum(eb1, axis=1, keepdims=True), jnp.sum(eb2, axis=1, keepdims=True)], axis=0
    )
    acc = jnp.concatenate(
        [
            jnp.dot(eb1.astype(jnp.bfloat16), vb1_ref[...], preferred_element_type=jnp.float32),
            jnp.dot(eb2.astype(jnp.bfloat16), vb2_ref[...], preferred_element_type=jnp.float32),
        ],
        axis=0,
    )
    for c in range(chunks):
        lo = c * KEY_CHUNK
        e = jnp.exp(s_ref[:, lo : lo + KEY_CHUNK] - high)
        tot = tot + jnp.sum(e, axis=1, keepdims=True)
        v = pg_ref[lo : lo + KEY_CHUNK, HEAD_SIZE : 2 * HEAD_SIZE]
        acc = acc + jnp.dot(e.astype(jnp.bfloat16), v, preferred_element_type=jnp.float32)
    res = (acc / tot).astype(jnp.bfloat16)
    o1_ref[...] = res[:rows]
    o2_ref[...] = res[rows:]


def attend_both(q1, kb1, vb1, q2, kb2, vb2, pages, usable):
    rows = q1.shape[0]
    keys_total = pages.shape[0]
    qspec = pl.BlockSpec((rows, HEAD_SIZE), lambda j: (0, j))
    full = pl.BlockSpec((rows, HEAD_SIZE), lambda j: (0, 0))
    return pl.pallas_call(
        attention_kernel,
        grid=(HEADS_PER_GROUP,),
        in_specs=[
            qspec,
            qspec,
            full,
            full,
            full,
            full,
            pl.BlockSpec((keys_total, 2 * HEAD_SIZE), lambda j: (0, 0)),
            pl.BlockSpec((1, keys_total), lambda j: (0, 0)),
        ],
        out_specs=[qspec, qspec],
        out_shape=[
            jax.ShapeDtypeStruct(q1.shape, jnp.bfloat16),
            jax.ShapeDtypeStruct(q1.shape, jnp.bfloat16),
        ],
        scratch_shapes=[pltpu.VMEM((2 * rows, keys_total), jnp.float32)],
        compiler_params=pltpu.CompilerParams(vmem_limit_bytes=48 * 1024 * 1024),
    )(q1, q2, kb1, vb1, kb2, vb2, pages, usable)


def body(
    embeddings,
    norm_gain,
    query_key_value_weight,
    embed_table,
    rotated_cache_pages,
    page_owner_device,
    cached_length,
    vocab_shard,
    shard_row,
    accept,
):
    members = lax.axis_size("tok")
    length = embeddings.shape[0]
    sources = jnp.arange(members, dtype=jnp.int32)
    positions = cached_length[0] + jnp.arange(length, dtype=jnp.int32)
    arrived = lax.all_to_all(rotated_cache_pages, "tok", split_axis=1, concat_axis=0, tiled=True)
    page_size = arrived.shape[2]
    pages = arrived.reshape(members * page_size, -1)
    page_index = jnp.sum(
        jnp.where(page_owner_device[0][:, None] == sources[None, :], sources[:, None], 0), axis=0
    )
    page_spots = page_index[:, None] * page_size + jnp.arange(page_size, dtype=jnp.int32)[None, :]
    usable = (page_spots.reshape(1, -1) < cached_length[0]).astype(jnp.float32)

    query_vectors, block_keys, block_values = project(
        embeddings, norm_gain, query_key_value_weight, positions
    )
    target_shard = vocab_shard[:, 0]
    capacity = max(2, 2 * length // members)
    chosen = (target_shard[:, None] == sources[None, :]).astype(jnp.int32)
    earlier = (jnp.arange(length)[:, None] > jnp.arange(length)[None, :]).astype(jnp.int32)
    slot_rank = jnp.sum(jnp.dot(earlier, chosen) * chosen, axis=1)
    slot_of = target_shard * capacity + slot_rank
    slots = jnp.arange(members * capacity, dtype=jnp.int32)
    wanted = jnp.sum(
        jnp.where(slot_of[:, None] == slots[None, :], shard_row[:, None], 0), axis=0
    ).reshape(members, capacity)
    asked = lax.all_to_all(wanted, "tok", split_axis=0, concat_axis=0, tiled=True)
    found_rows = jnp.take(embed_table, asked, axis=0)
    returned = lax.all_to_all(found_rows, "tok", split_axis=0, concat_axis=0, tiled=True)
    replacement = returned[target_shard, slot_rank]
    full_rows = lax.all_gather(replacement, "head", axis=1, tiled=True)
    replaced = jnp.where(accept[:, None] == 1, full_rows, embeddings)
    queries_two, keys_two, values_two = project(
        replaced, norm_gain, query_key_value_weight, positions
    )
    return attend_both(
        query_vectors, block_keys, block_values, queries_two, keys_two, values_two, pages, usable
    )


def solution(mesh):
    return jax.shard_map(
        body,
        mesh=mesh,
        in_specs=(
            P("tok", None),
            P(),
            P(None, "head"),
            P("tok", "head"),
            P("tok", None, None, "head"),
            P("tok", None),
            P("tok"),
            P("tok", None),
            P("tok"),
            P("tok"),
        ),
        out_specs=(P("tok", "head"), P("tok", "head")),
        check_vma=False,
    )
```

```python
import math

import jax
import jax.numpy as jnp
from jax import lax
from jax.experimental import pallas as pl
from jax.experimental.pallas import tpu as pltpu
from jax.sharding import PartitionSpec as P

QUERY_HEADS = 32
KEY_VALUE_HEADS = 8
HEAD_SIZE = 128
HEADS_PER_GROUP = QUERY_HEADS // KEY_VALUE_HEADS


THETA = 500000.0
KEY_CHUNK = 1024


def angles(positions):
    steps_half = jnp.arange(HEAD_SIZE // 2, dtype=jnp.float32)
    frequency = THETA ** (-(steps_half * 2.0) / HEAD_SIZE)
    return positions.astype(jnp.float32)[:, None] * frequency[None, :]


def rotate(vectors, turning):
    half_width = vectors.shape[-1] // 2
    former = vectors[..., :half_width]
    latter = vectors[..., half_width:]
    cosine = jnp.cos(turning)
    sine_of = jnp.sin(turning)
    return jnp.concatenate(
        [former * cosine - latter * sine_of, latter * cosine + former * sine_of], axis=-1
    )


def project(inputs, norm_gain, query_key_value_weight, positions):
    widened = inputs.astype(jnp.float32)
    inverse = lax.rsqrt(jnp.mean(widened * widened, axis=-1, keepdims=True) + 1e-05)
    normed = (widened * inverse * norm_gain.astype(jnp.float32)).astype(jnp.bfloat16)
    combined = jnp.dot(normed, query_key_value_weight, preferred_element_type=jnp.float32)
    rows = inputs.shape[0]
    combined = combined.reshape(rows, -1, HEADS_PER_GROUP + 2, HEAD_SIZE)
    turning = angles(positions)[:, None, None, :]
    query_vectors = rotate(combined[:, :, :HEADS_PER_GROUP], turning).astype(jnp.bfloat16)
    block_keys = rotate(combined[:, :, HEADS_PER_GROUP : HEADS_PER_GROUP + 1], turning)[
        :, :, 0
    ].astype(jnp.bfloat16)
    block_values = combined[:, :, HEADS_PER_GROUP + 1].astype(jnp.bfloat16)
    return (
        query_vectors.reshape(rows, -1),
        block_keys.reshape(rows, -1),
        block_values.reshape(rows, -1),
    )


def attention_kernel(q1_ref, q2_ref, kb1_ref, vb1_ref, kb2_ref, vb2_ref, pg_ref, us_ref,
                     o1_ref, o2_ref, s_ref):
    factor = 1.0 / math.sqrt(HEAD_SIZE)
    nt = (((1,), (1,)), ((), ()))
    rows = q1_ref.shape[0]
    q = jnp.concatenate([q1_ref[...], q2_ref[...]], axis=0)
    sb1 = lax.dot_general(q1_ref[...], kb1_ref[...], nt, preferred_element_type=jnp.float32) * factor
    sb2 = lax.dot_general(q2_ref[...], kb2_ref[...], nt, preferred_element_type=jnp.float32) * factor
    high = jnp.concatenate(
        [jnp.max(sb1, axis=1, keepdims=True), jnp.max(sb2, axis=1, keepdims=True)], axis=0
    )
    keys_total = pg_ref.shape[0]
    chunks = keys_total // KEY_CHUNK
    for c in range(chunks):
        lo = c * KEY_CHUNK
        k = pg_ref[lo : lo + KEY_CHUNK, 0:HEAD_SIZE]
        sc = lax.dot_general(q, k, nt, preferred_element_type=jnp.float32) * factor
        sc = jnp.where(us_ref[:, lo : lo + KEY_CHUNK] > 0, sc, -1e30)
        s_ref[:, lo : lo + KEY_CHUNK] = sc
        high = jnp.maximum(high, jnp.max(sc, axis=1, keepdims=True))
    h1 = high[:rows]
    h2 = high[rows:]
    eb1 = jnp.exp(sb1 - h1)
    eb2 = jnp.exp(sb2 - h2)
    tot = jnp.concatenate(
        [jnp.sum(eb1, axis=1, keepdims=True), jnp.sum(eb2, axis=1, keepdims=True)], axis=0
    )
    acc = jnp.concatenate(
        [
            jnp.dot(eb1.astype(jnp.bfloat16), vb1_ref[...], preferred_element_type=jnp.float32),
            jnp.dot(eb2.astype(jnp.bfloat16), vb2_ref[...], preferred_element_type=jnp.float32),
        ],
        axis=0,
    )
    for c in range(chunks):
        lo = c * KEY_CHUNK
        e = jnp.exp(s_ref[:, lo : lo + KEY_CHUNK] - high)
        tot = tot + jnp.sum(e, axis=1, keepdims=True)
        v = pg_ref[lo : lo + KEY_CHUNK, HEAD_SIZE : 2 * HEAD_SIZE]
        acc = acc + jnp.dot(e.astype(jnp.bfloat16), v, preferred_element_type=jnp.float32)
    res = (acc / tot).astype(jnp.bfloat16)
    o1_ref[...] = res[:rows]
    o2_ref[...] = res[rows:]


def attend_both(q1, kb1, vb1, q2, kb2, vb2, pages, usable):
    rows = q1.shape[0]
    keys_total = pages.shape[0]
    qspec = pl.BlockSpec((rows, HEAD_SIZE), lambda j: (0, j))
    full = pl.BlockSpec((rows, HEAD_SIZE), lambda j: (0, 0))
    return pl.pallas_call(
        attention_kernel,
        grid=(HEADS_PER_GROUP,),
        in_specs=[
            qspec,
            qspec,
            full,
            full,
            full,
            full,
            pl.BlockSpec((keys_total, 2 * HEAD_SIZE), lambda j: (0, 0)),
            pl.BlockSpec((1, keys_total), lambda j: (0, 0)),
        ],
        out_specs=[qspec, qspec],
        out_shape=[
            jax.ShapeDtypeStruct(q1.shape, jnp.bfloat16),
            jax.ShapeDtypeStruct(q1.shape, jnp.bfloat16),
        ],
        scratch_shapes=[pltpu.VMEM((2 * rows, keys_total), jnp.float32)],
        compiler_params=pltpu.CompilerParams(vmem_limit_bytes=48 * 1024 * 1024),
    )(q1, q2, kb1, vb1, kb2, vb2, pages, usable)


def body(
    embeddings,
    norm_gain,
    query_key_value_weight,
    embed_table,
    rotated_cache_pages,
    page_owner_device,
    cached_length,
    vocab_shard,
    shard_row,
    accept,
):
    members = lax.axis_size("tok")
    length = embeddings.shape[0]
    sources = jnp.arange(members, dtype=jnp.int32)
    positions = cached_length[0] + jnp.arange(length, dtype=jnp.int32)
    arrived = lax.all_to_all(rotated_cache_pages, "tok", split_axis=1, concat_axis=0, tiled=True)
    page_size = arrived.shape[2]
    pages = arrived.reshape(members * page_size, -1)
    page_index = jnp.sum(
        jnp.where(page_owner_device[0][:, None] == sources[None, :], sources[:, None], 0), axis=0
    )
    page_spots = page_index[:, None] * page_size + jnp.arange(page_size, dtype=jnp.int32)[None, :]
    usable = (page_spots.reshape(1, -1) < cached_length[0]).astype(jnp.float32)

    query_vectors, block_keys, block_values = project(
        embeddings, norm_gain, query_key_value_weight, positions
    )
    target_shard = vocab_shard[:, 0]
    most = members
    taken = accept == 1
    order = jnp.cumsum(taken.astype(jnp.int32)) - 1
    slots = jnp.arange(most, dtype=jnp.int32)
    hit = taken[:, None] & (order[:, None] == slots[None, :])
    filled = jnp.any(hit, axis=0)
    req_shard = jnp.where(filled, jnp.sum(jnp.where(hit, target_shard[:, None], 0), axis=0), -1)
    req_row = jnp.sum(jnp.where(hit, shard_row[:, None], 0), axis=0)
    request = jnp.stack([req_shard, req_row]).astype(jnp.float32)
    request = jnp.pad(request, ((0, 0), (0, 512 - most)))
    me = lax.axis_index("tok")
    placed = jnp.where((sources == me)[:, None, None], request[None], jnp.zeros((), request.dtype))
    every_request = lax.psum(placed, "tok")
    from_here = every_request[:, 0, :most].astype(jnp.int32) == me
    rows_here = jnp.clip(every_request[:, 1, :most].astype(jnp.int32), 0, embed_table.shape[0] - 1)
    looked = jnp.take(embed_table, rows_here.reshape(-1), axis=0).reshape(
        members, most, embed_table.shape[1]
    )
    looked = jnp.where(from_here[:, :, None], looked, jnp.zeros((), looked.dtype))
    mine = lax.psum_scatter(looked, "tok", scatter_dimension=0, tiled=True)[0]
    group = lax.axis_index("head")
    groups = lax.axis_size("head")
    spread = jnp.where(
        (jnp.arange(groups) == group)[None, :, None],
        mine[:, None, :],
        jnp.zeros((), mine.dtype),
    )
    full_rows = lax.psum(spread, "head").reshape(mine.shape[0], -1)
    picked = jnp.take(full_rows, jnp.clip(order, 0, most - 1), axis=0)
    replaced = jnp.where(taken[:, None], picked, embeddings)
    queries_two, keys_two, values_two = project(
        replaced, norm_gain, query_key_value_weight, positions
    )
    return attend_both(
        query_vectors, block_keys, block_values, queries_two, keys_two, values_two, pages, usable
    )


def solution(mesh):
    return jax.shard_map(
        body,
        mesh=mesh,
        in_specs=(
            P("tok", None),
            P(),
            P(None, "head"),
            P("tok", "head"),
            P("tok", None, None, "head"),
            P("tok", None),
            P("tok"),
            P("tok", None),
            P("tok"),
            P("tok"),
        ),
        out_specs=(P("tok", "head"), P("tok", "head")),
        check_vma=False,
    )
```

```python
import math

import jax
import jax.numpy as jnp
from jax import lax
from jax.experimental import pallas as pl
from jax.experimental.pallas import tpu as pltpu
from jax.sharding import PartitionSpec as P


QUERY_HEADS = 32
KEY_VALUE_HEADS = 8
HEAD_SIZE = 128
HEADS_PER_GROUP = QUERY_HEADS // KEY_VALUE_HEADS


THETA = 500000.0
PAGE_ROWS = 256
ID_ROWS = 8
ID_SPLIT = 64


def angles(positions):
    steps_half = jnp.arange(HEAD_SIZE // 2, dtype=jnp.float32)
    frequency = THETA ** (-(steps_half * 2.0) / HEAD_SIZE)
    return positions.astype(jnp.float32)[:, None] * frequency[None, :]


def rotate(vectors, turning):
    half_width = vectors.shape[-1] // 2
    former = vectors[..., :half_width]
    latter = vectors[..., half_width:]
    cosine = jnp.cos(turning)
    sine_of = jnp.sin(turning)
    return jnp.concatenate(
        [former * cosine - latter * sine_of, latter * cosine + former * sine_of], axis=-1
    )


def project(inputs, norm_gain, query_key_value_weight, positions, turning=None):
    widened = inputs.astype(jnp.float32)
    inverse = lax.rsqrt(jnp.mean(widened * widened, axis=-1, keepdims=True) + 1e-05)
    normed = (widened * inverse * norm_gain.astype(jnp.float32)).astype(jnp.bfloat16)
    combined = jnp.dot(normed, query_key_value_weight, preferred_element_type=jnp.float32)
    rows = inputs.shape[0]
    combined = combined.reshape(rows, -1, HEADS_PER_GROUP + 2, HEAD_SIZE)
    if turning is None:
        turning = angles(positions)
    turning = turning[:, None, None, :]
    query_vectors = rotate(combined[:, :, :HEADS_PER_GROUP], turning).astype(jnp.bfloat16)
    block_keys = rotate(combined[:, :, HEADS_PER_GROUP : HEADS_PER_GROUP + 1], turning)[
        :, :, 0
    ].astype(jnp.bfloat16)
    block_values = combined[:, :, HEADS_PER_GROUP + 1].astype(jnp.bfloat16)
    return (
        query_vectors.reshape(rows, -1),
        block_keys.reshape(rows, -1),
        block_values.reshape(rows, -1),
    )


def attention_kernel(q_ref, kb_ref, vb_ref, us_ref, pg_ref, o_ref, s_ref):
    factor = 1.0 / math.sqrt(HEAD_SIZE)
    nt = (((1,), (1,)), ((), ()))
    q = q_ref[...]
    sb = lax.dot_general(q, kb_ref[...], nt, preferred_element_type=jnp.float32) * factor
    high = jnp.max(sb, axis=1, keepdims=True)
    sources = pg_ref.shape[0]
    chunk = PAGE_ROWS
    for c in range(sources):
        lo = c * chunk
        k = pg_ref[c, 0:chunk, 0:HEAD_SIZE]
        sc = lax.dot_general(q, k, nt, preferred_element_type=jnp.float32) * factor
        sc = jnp.where(us_ref[:, lo : lo + chunk] > 0, sc, -1e30)
        s_ref[:, lo : lo + chunk] = sc
        high = jnp.maximum(high, jnp.max(sc, axis=1, keepdims=True))
    eb = jnp.exp(sb - high)
    tot = jnp.sum(eb, axis=1, keepdims=True)
    acc = jnp.dot(eb.astype(jnp.bfloat16), vb_ref[...], preferred_element_type=jnp.float32)
    for c in range(sources):
        lo = c * chunk
        e = jnp.exp(s_ref[:, lo : lo + chunk] - high)
        tot = tot + jnp.sum(e, axis=1, keepdims=True)
        v = pg_ref[c, 0:chunk, HEAD_SIZE : 2 * HEAD_SIZE]
        acc = acc + jnp.dot(e.astype(jnp.bfloat16), v, preferred_element_type=jnp.float32)
    o_ref[...] = (acc / tot).astype(jnp.bfloat16)


def attend_one(q, kb, vb, pages, usable):
    rows = q.shape[0]
    keys_total = usable.shape[1]
    qspec = pl.BlockSpec((rows, HEAD_SIZE), lambda j: (0, j))
    full = pl.BlockSpec((rows, HEAD_SIZE), lambda j: (0, 0))
    return pl.pallas_call(
        attention_kernel,
        grid=(HEADS_PER_GROUP,),
        in_specs=[
            qspec,
            full,
            full,
            pl.BlockSpec((1, keys_total), lambda j: (0, 0)),
            pl.BlockSpec(pages.shape, lambda j: (0, 0, 0)),
        ],
        out_specs=qspec,
        out_shape=jax.ShapeDtypeStruct(q.shape, jnp.bfloat16),
        scratch_shapes=[pltpu.VMEM((rows, keys_total), jnp.float32)],
        compiler_params=pltpu.CompilerParams(vmem_limit_bytes=48 * 1024 * 1024),
    )(q, kb, vb, usable, pages)


def body(
    embeddings,
    norm_gain,
    query_key_value_weight,
    embed_table,
    rotated_cache_pages,
    page_owner_device,
    cached_length,
    vocab_shard,
    shard_row,
    accept,
):
    members = lax.axis_size("tok")
    length = embeddings.shape[0]
    sources = jnp.arange(members, dtype=jnp.int32)
    positions = cached_length[0] + jnp.arange(length, dtype=jnp.int32)

    own_rows, own_gain, own_turning = lax.optimization_barrier(
        (embeddings, norm_gain, angles(positions))
    )
    query_vectors, block_keys, block_values = lax.optimization_barrier(
        project(own_rows, own_gain, query_key_value_weight, None, own_turning)
    )
    target_shard = vocab_shard[:, 0]
    capacity = max(2, 2 * length // members)
    chosen = (target_shard[:, None] == sources[None, :]).astype(jnp.int32)
    earlier = (jnp.arange(length)[:, None] > jnp.arange(length)[None, :]).astype(jnp.int32)
    slot_rank = jnp.sum(jnp.dot(earlier, chosen) * chosen, axis=1)
    slot_of = target_shard * capacity + slot_rank
    slots = jnp.arange(members * capacity, dtype=jnp.int32)
    wanted = jnp.sum(
        jnp.where(slot_of[:, None] == slots[None, :], shard_row[:, None], 0), axis=0
    ).reshape(members, capacity)
    lanes = rotated_cache_pages.shape[3]
    coded = jnp.concatenate([wanted // ID_SPLIT, wanted % ID_SPLIT], axis=1).astype(jnp.bfloat16)
    coded = jnp.pad(coded, ((0, 0), (0, lanes - coded.shape[1])))
    coded = jnp.broadcast_to(coded[:, None, :], (members, ID_ROWS, lanes))
    outgoing = jnp.concatenate([rotated_cache_pages[0], coded], axis=1)[None]
    arrived = lax.all_to_all(outgoing, "tok", split_axis=1, concat_axis=0, tiled=True)[:, 0]
    page_size = rotated_cache_pages.shape[2]
    ids_in = arrived[:, page_size, : 2 * capacity].astype(jnp.int32)
    asked = ids_in[:, :capacity] * ID_SPLIT + ids_in[:, capacity:]

    page_index = jnp.sum(
        jnp.where(page_owner_device[0][:, None] == sources[None, :], sources[:, None], 0), axis=0
    )
    page_spots = page_index[:, None] * page_size + jnp.arange(page_size, dtype=jnp.int32)[None, :]
    usable = (page_spots.reshape(1, -1) < cached_length[0]).astype(jnp.float32)

    output_one = attend_one(query_vectors, block_keys, block_values, arrived, usable)
    found_rows = jnp.take(embed_table, asked, axis=0)
    returned = lax.all_to_all(found_rows, "tok", split_axis=0, concat_axis=0, tiled=True)
    taken = accept == 1
    most = members
    order = jnp.cumsum(taken.astype(jnp.int32)) - 1
    compact_slots = jnp.arange(most, dtype=jnp.int32)
    hit = taken[:, None] & (order[:, None] == compact_slots[None, :])
    token_of = jnp.sum(jnp.where(hit, jnp.arange(length, dtype=jnp.int32)[:, None], 0), axis=0)
    compact = returned[target_shard[token_of], slot_rank[token_of]]
    full_rows = lax.all_gather(compact, "head", axis=1, tiled=True)
    picked = jnp.take(full_rows, jnp.clip(order, 0, most - 1), axis=0)
    replaced = jnp.where(taken[:, None], picked, embeddings)
    queries_two, keys_two, values_two = project(
        replaced, norm_gain, query_key_value_weight, positions
    )
    output_two = attend_one(queries_two, keys_two, values_two, arrived, usable)
    return output_one, output_two


def solution(mesh):
    return jax.shard_map(
        body,
        mesh=mesh,
        in_specs=(
            P("tok", None),
            P(),
            P(None, "head"),
            P("tok", "head"),
            P("tok", None, None, "head"),
            P("tok", None),
            P("tok"),
            P("tok", None),
            P("tok"),
            P("tok"),
        ),
        out_specs=(P("tok", "head"), P("tok", "head")),
        check_vma=False,
    )
```

```python
import math

import jax
import jax.numpy as jnp
from jax import lax
from jax.experimental import pallas as pl
from jax.experimental.pallas import tpu as pltpu
from jax.sharding import PartitionSpec as P

QUERY_HEADS = 32
KEY_VALUE_HEADS = 8
HEAD_SIZE = 128
HEADS_PER_GROUP = QUERY_HEADS // KEY_VALUE_HEADS


THETA = 500000.0
KEY_CHUNK = 1024


def angles(positions):
    steps_half = jnp.arange(HEAD_SIZE // 2, dtype=jnp.float32)
    frequency = THETA ** (-(steps_half * 2.0) / HEAD_SIZE)
    return positions.astype(jnp.float32)[:, None] * frequency[None, :]


def rotate(vectors, turning):
    half_width = vectors.shape[-1] // 2
    former = vectors[..., :half_width]
    latter = vectors[..., half_width:]
    cosine = jnp.cos(turning)
    sine_of = jnp.sin(turning)
    return jnp.concatenate(
        [former * cosine - latter * sine_of, latter * cosine + former * sine_of], axis=-1
    )


def project(inputs, norm_gain, query_key_value_weight, positions):
    widened = inputs.astype(jnp.float32)
    inverse = lax.rsqrt(jnp.mean(widened * widened, axis=-1, keepdims=True) + 1e-05)
    normed = (widened * inverse * norm_gain.astype(jnp.float32)).astype(jnp.bfloat16)
    combined = jnp.dot(normed, query_key_value_weight, preferred_element_type=jnp.float32)
    rows = inputs.shape[0]
    combined = combined.reshape(rows, -1, HEADS_PER_GROUP + 2, HEAD_SIZE)
    turning = angles(positions)[:, None, None, :]
    query_vectors = rotate(combined[:, :, :HEADS_PER_GROUP], turning).astype(jnp.bfloat16)
    block_keys = rotate(combined[:, :, HEADS_PER_GROUP : HEADS_PER_GROUP + 1], turning)[
        :, :, 0
    ].astype(jnp.bfloat16)
    block_values = combined[:, :, HEADS_PER_GROUP + 1].astype(jnp.bfloat16)
    return (
        query_vectors.reshape(rows, -1),
        block_keys.reshape(rows, -1),
        block_values.reshape(rows, -1),
    )


def attention_kernel(q1_ref, q2_ref, kb1_ref, vb1_ref, kb2_ref, vb2_ref, pg_ref, us_ref,
                     o1_ref, o2_ref, s_ref):
    factor = 1.0 / math.sqrt(HEAD_SIZE)
    nt = (((1,), (1,)), ((), ()))
    rows = q1_ref.shape[0]
    q = jnp.concatenate([q1_ref[...], q2_ref[...]], axis=0)
    sb1 = lax.dot_general(q1_ref[...], kb1_ref[...], nt, preferred_element_type=jnp.float32) * factor
    sb2 = lax.dot_general(q2_ref[...], kb2_ref[...], nt, preferred_element_type=jnp.float32) * factor
    lanes = HEAD_SIZE
    high_part = jnp.concatenate([sb1, sb2], axis=0)
    keys_total = pg_ref.shape[0]
    chunks = keys_total // KEY_CHUNK
    for c in range(chunks):
        lo = c * KEY_CHUNK
        k = pg_ref[lo : lo + KEY_CHUNK, 0:HEAD_SIZE]
        sc = lax.dot_general(q, k, nt, preferred_element_type=jnp.float32) * factor
        sc = jnp.where(us_ref[:, lo : lo + KEY_CHUNK] > 0, sc, -1e30)
        s_ref[:, lo : lo + KEY_CHUNK] = sc
        for j in range(KEY_CHUNK // lanes):
            high_part = jnp.maximum(high_part, sc[:, j * lanes : (j + 1) * lanes])
    high = jnp.max(high_part, axis=1, keepdims=True)
    h1 = high[:rows]
    h2 = high[rows:]
    eb1 = jnp.exp(sb1 - h1)
    eb2 = jnp.exp(sb2 - h2)
    tot_part = jnp.concatenate([eb1, eb2], axis=0)
    acc = jnp.concatenate(
        [
            jnp.dot(eb1.astype(jnp.bfloat16), vb1_ref[...], preferred_element_type=jnp.float32),
            jnp.dot(eb2.astype(jnp.bfloat16), vb2_ref[...], preferred_element_type=jnp.float32),
        ],
        axis=0,
    )
    for c in range(chunks):
        lo = c * KEY_CHUNK
        e = jnp.exp(s_ref[:, lo : lo + KEY_CHUNK] - high)
        for j in range(KEY_CHUNK // lanes):
            tot_part = tot_part + e[:, j * lanes : (j + 1) * lanes]
        v = pg_ref[lo : lo + KEY_CHUNK, HEAD_SIZE : 2 * HEAD_SIZE]
        acc = acc + jnp.dot(e.astype(jnp.bfloat16), v, preferred_element_type=jnp.float32)
    tot = jnp.sum(tot_part, axis=1, keepdims=True)
    res = (acc / tot).astype(jnp.bfloat16)
    o1_ref[...] = res[:rows]
    o2_ref[...] = res[rows:]


def attend_both(q1, kb1, vb1, q2, kb2, vb2, pages, usable):
    rows = q1.shape[0]
    keys_total = pages.shape[0]
    qspec = pl.BlockSpec((rows, HEAD_SIZE), lambda j: (0, j))
    full = pl.BlockSpec((rows, HEAD_SIZE), lambda j: (0, 0))
    return pl.pallas_call(
        attention_kernel,
        grid=(HEADS_PER_GROUP,),
        in_specs=[
            qspec,
            qspec,
            full,
            full,
            full,
            full,
            pl.BlockSpec((keys_total, 2 * HEAD_SIZE), lambda j: (0, 0)),
            pl.BlockSpec((1, keys_total), lambda j: (0, 0)),
        ],
        out_specs=[qspec, qspec],
        out_shape=[
            jax.ShapeDtypeStruct(q1.shape, jnp.bfloat16),
            jax.ShapeDtypeStruct(q1.shape, jnp.bfloat16),
        ],
        scratch_shapes=[pltpu.VMEM((2 * rows, keys_total), jnp.float32)],
        compiler_params=pltpu.CompilerParams(vmem_limit_bytes=48 * 1024 * 1024),
    )(q1, q2, kb1, vb1, kb2, vb2, pages, usable)


def body(
    embeddings,
    norm_gain,
    query_key_value_weight,
    embed_table,
    rotated_cache_pages,
    page_owner_device,
    cached_length,
    vocab_shard,
    shard_row,
    accept,
):
    members = lax.axis_size("tok")
    length = embeddings.shape[0]
    sources = jnp.arange(members, dtype=jnp.int32)
    positions = cached_length[0] + jnp.arange(length, dtype=jnp.int32)
    page_size = rotated_cache_pages.shape[2]
    page_index = jnp.sum(
        jnp.where(page_owner_device[0][:, None] == sources[None, :], sources[:, None], 0), axis=0
    )
    page_spots = page_index[:, None] * page_size + jnp.arange(page_size, dtype=jnp.int32)[None, :]
    usable = (page_spots.reshape(1, -1) < cached_length[0]).astype(jnp.float32)

    query_vectors, block_keys, block_values = project(
        embeddings, norm_gain, query_key_value_weight, positions
    )
    target_shard = vocab_shard[:, 0]
    capacity = max(2, 2 * length // members)
    chosen = (target_shard[:, None] == sources[None, :]).astype(jnp.int32)
    earlier = (jnp.arange(length)[:, None] > jnp.arange(length)[None, :]).astype(jnp.int32)
    slot_rank = jnp.sum(jnp.dot(earlier, chosen) * chosen, axis=1)
    slot_of = target_shard * capacity + slot_rank
    slots = jnp.arange(members * capacity, dtype=jnp.int32)
    wanted = jnp.sum(
        jnp.where(slot_of[:, None] == slots[None, :], shard_row[:, None], 0), axis=0
    ).reshape(members, capacity)
    asked = lax.all_to_all(wanted, "tok", split_axis=0, concat_axis=0, tiled=True)
    found_rows = jnp.take(embed_table, asked, axis=0)
    returned = lax.all_to_all(found_rows, "tok", split_axis=0, concat_axis=0, tiled=True)
    taken = accept == 1
    most = members
    order = jnp.cumsum(taken.astype(jnp.int32)) - 1
    slots = jnp.arange(most, dtype=jnp.int32)
    hit = taken[:, None] & (order[:, None] == slots[None, :])
    token_of = jnp.sum(jnp.where(hit, jnp.arange(length, dtype=jnp.int32)[:, None], 0), axis=0)
    compact = returned[target_shard[token_of], slot_rank[token_of]]
    full_rows = lax.all_gather(compact, "head", axis=1, tiled=True)
    picked = jnp.take(full_rows, jnp.clip(order, 0, most - 1), axis=0)
    replaced = jnp.where(taken[:, None], picked, embeddings)
    arrived = lax.all_to_all(rotated_cache_pages, "tok", split_axis=1, concat_axis=0, tiled=True)
    page_size = arrived.shape[2]
    pages = arrived.reshape(members * page_size, -1)
    queries_two, keys_two, values_two = project(
        replaced, norm_gain, query_key_value_weight, positions
    )
    return attend_both(
        query_vectors, block_keys, block_values, queries_two, keys_two, values_two, pages, usable
    )


def solution(mesh):
    return jax.shard_map(
        body,
        mesh=mesh,
        in_specs=(
            P("tok", None),
            P(),
            P(None, "head"),
            P("tok", "head"),
            P("tok", None, None, "head"),
            P("tok", None),
            P("tok"),
            P("tok", None),
            P("tok"),
            P("tok"),
        ),
        out_specs=(P("tok", "head"), P("tok", "head")),
        check_vma=False,
    )
```

```python
import math

import jax
import jax.numpy as jnp
from jax import lax
from jax.experimental import pallas as pl
from jax.experimental.pallas import tpu as pltpu
from jax.sharding import PartitionSpec as P

QUERY_HEADS = 32
KEY_VALUE_HEADS = 8
HEAD_SIZE = 128
HEADS_PER_GROUP = QUERY_HEADS // KEY_VALUE_HEADS


THETA = 500000.0
KEY_CHUNK = 1024


def angles(positions):
    steps_half = jnp.arange(HEAD_SIZE // 2, dtype=jnp.float32)
    frequency = THETA ** (-(steps_half * 2.0) / HEAD_SIZE)
    return positions.astype(jnp.float32)[:, None] * frequency[None, :]


def rotate(vectors, turning):
    half_width = vectors.shape[-1] // 2
    former = vectors[..., :half_width]
    latter = vectors[..., half_width:]
    cosine = jnp.cos(turning)
    sine_of = jnp.sin(turning)
    return jnp.concatenate(
        [former * cosine - latter * sine_of, latter * cosine + former * sine_of], axis=-1
    )


def project(inputs, norm_gain, query_key_value_weight, positions):
    widened = inputs.astype(jnp.float32)
    inverse = lax.rsqrt(jnp.mean(widened * widened, axis=-1, keepdims=True) + 1e-05)
    normed = (widened * inverse * norm_gain.astype(jnp.float32)).astype(jnp.bfloat16)
    combined = jnp.dot(normed, query_key_value_weight, preferred_element_type=jnp.float32)
    rows = inputs.shape[0]
    combined = combined.reshape(rows, -1, HEADS_PER_GROUP + 2, HEAD_SIZE)
    turning = angles(positions)[:, None, None, :]
    query_vectors = rotate(combined[:, :, :HEADS_PER_GROUP], turning).astype(jnp.bfloat16)
    block_keys = rotate(combined[:, :, HEADS_PER_GROUP : HEADS_PER_GROUP + 1], turning)[
        :, :, 0
    ].astype(jnp.bfloat16)
    block_values = combined[:, :, HEADS_PER_GROUP + 1].astype(jnp.bfloat16)
    return (
        query_vectors.reshape(rows, -1),
        block_keys.reshape(rows, -1),
        block_values.reshape(rows, -1),
    )


def attention_kernel(full_ref, q1_ref, q2_ref, kb1_ref, vb1_ref, kb2_ref, vb2_ref, pg_ref, us_ref,
                     o1_ref, o2_ref, s_ref):
    factor = 1.0 / math.sqrt(HEAD_SIZE)
    nt = (((1,), (1,)), ((), ()))
    rows = q1_ref.shape[0]
    q = jnp.concatenate([q1_ref[...], q2_ref[...]], axis=0)
    sb1 = lax.dot_general(q1_ref[...], kb1_ref[...], nt, preferred_element_type=jnp.float32) * factor
    sb2 = lax.dot_general(q2_ref[...], kb2_ref[...], nt, preferred_element_type=jnp.float32) * factor
    high = jnp.concatenate(
        [jnp.max(sb1, axis=1, keepdims=True), jnp.max(sb2, axis=1, keepdims=True)], axis=0
    )
    keys_total = pg_ref.shape[0]
    chunks = keys_total // KEY_CHUNK
    for c in range(chunks):
        lo = c * KEY_CHUNK
        k = pg_ref[lo : lo + KEY_CHUNK, 0:HEAD_SIZE]
        sc = lax.dot_general(q, k, nt, preferred_element_type=jnp.float32) * factor
        s_ref[:, lo : lo + KEY_CHUNK] = sc

        @pl.when(full_ref[c] == 0)
        def _():
            s_ref[:, lo : lo + KEY_CHUNK] = jnp.where(
                us_ref[:, lo : lo + KEY_CHUNK] > 0, s_ref[:, lo : lo + KEY_CHUNK], -1e30
            )

        high = jnp.maximum(high, jnp.max(s_ref[:, lo : lo + KEY_CHUNK], axis=1, keepdims=True))
    h1 = high[:rows]
    h2 = high[rows:]
    eb1 = jnp.exp(sb1 - h1)
    eb2 = jnp.exp(sb2 - h2)
    tot = jnp.concatenate(
        [jnp.sum(eb1, axis=1, keepdims=True), jnp.sum(eb2, axis=1, keepdims=True)], axis=0
    )
    acc = jnp.concatenate(
        [
            jnp.dot(eb1.astype(jnp.bfloat16), vb1_ref[...], preferred_element_type=jnp.float32),
            jnp.dot(eb2.astype(jnp.bfloat16), vb2_ref[...], preferred_element_type=jnp.float32),
        ],
        axis=0,
    )
    for c in range(chunks):
        lo = c * KEY_CHUNK
        e = jnp.exp(s_ref[:, lo : lo + KEY_CHUNK] - high)
        tot = tot + jnp.sum(e, axis=1, keepdims=True)
        v = pg_ref[lo : lo + KEY_CHUNK, HEAD_SIZE : 2 * HEAD_SIZE]
        acc = acc + jnp.dot(e.astype(jnp.bfloat16), v, preferred_element_type=jnp.float32)
    res = (acc / tot).astype(jnp.bfloat16)
    o1_ref[...] = res[:rows]
    o2_ref[...] = res[rows:]


def attend_both(q1, kb1, vb1, q2, kb2, vb2, pages, usable):
    rows = q1.shape[0]
    keys_total = pages.shape[0]
    qspec = pl.BlockSpec((rows, HEAD_SIZE), lambda j, f: (0, j))
    full = pl.BlockSpec((rows, HEAD_SIZE), lambda j, f: (0, 0))
    chunk_full = jnp.min(usable.reshape(-1, KEY_CHUNK), axis=1).astype(jnp.int32)
    grid_spec = pltpu.PrefetchScalarGridSpec(
        num_scalar_prefetch=1,
        grid=(HEADS_PER_GROUP,),
        in_specs=[
            qspec,
            qspec,
            full,
            full,
            full,
            full,
            pl.BlockSpec((keys_total, 2 * HEAD_SIZE), lambda j, f: (0, 0)),
            pl.BlockSpec((1, keys_total), lambda j, f: (0, 0)),
        ],
        out_specs=[qspec, qspec],
        scratch_shapes=[pltpu.VMEM((2 * rows, keys_total), jnp.float32)],
    )
    return pl.pallas_call(
        attention_kernel,
        grid_spec=grid_spec,
        out_shape=[
            jax.ShapeDtypeStruct(q1.shape, jnp.bfloat16),
            jax.ShapeDtypeStruct(q1.shape, jnp.bfloat16),
        ],
        compiler_params=pltpu.CompilerParams(vmem_limit_bytes=48 * 1024 * 1024),
    )(chunk_full, q1, q2, kb1, vb1, kb2, vb2, pages, usable)


def body(
    embeddings,
    norm_gain,
    query_key_value_weight,
    embed_table,
    rotated_cache_pages,
    page_owner_device,
    cached_length,
    vocab_shard,
    shard_row,
    accept,
):
    members = lax.axis_size("tok")
    length = embeddings.shape[0]
    sources = jnp.arange(members, dtype=jnp.int32)
    positions = cached_length[0] + jnp.arange(length, dtype=jnp.int32)
    page_size = rotated_cache_pages.shape[2]
    page_index = jnp.sum(
        jnp.where(page_owner_device[0][:, None] == sources[None, :], sources[:, None], 0), axis=0
    )
    page_spots = page_index[:, None] * page_size + jnp.arange(page_size, dtype=jnp.int32)[None, :]
    usable = (page_spots.reshape(1, -1) < cached_length[0]).astype(jnp.float32)

    query_vectors, block_keys, block_values = project(
        embeddings, norm_gain, query_key_value_weight, positions
    )
    target_shard = vocab_shard[:, 0]
    capacity = max(2, 2 * length // members)
    chosen = (target_shard[:, None] == sources[None, :]).astype(jnp.int32)
    earlier = (jnp.arange(length)[:, None] > jnp.arange(length)[None, :]).astype(jnp.int32)
    slot_rank = jnp.sum(jnp.dot(earlier, chosen) * chosen, axis=1)
    slot_of = target_shard * capacity + slot_rank
    slots = jnp.arange(members * capacity, dtype=jnp.int32)
    wanted = jnp.sum(
        jnp.where(slot_of[:, None] == slots[None, :], shard_row[:, None], 0), axis=0
    ).reshape(members, capacity)
    asked = lax.all_to_all(wanted, "tok", split_axis=0, concat_axis=0, tiled=True)
    found_rows = jnp.take(embed_table, asked, axis=0)
    returned = lax.all_to_all(found_rows, "tok", split_axis=0, concat_axis=0, tiled=True)
    taken = accept == 1
    most = members
    order = jnp.cumsum(taken.astype(jnp.int32)) - 1
    slots = jnp.arange(most, dtype=jnp.int32)
    hit = taken[:, None] & (order[:, None] == slots[None, :])
    token_of = jnp.sum(jnp.where(hit, jnp.arange(length, dtype=jnp.int32)[:, None], 0), axis=0)
    compact = returned[target_shard[token_of], slot_rank[token_of]]
    full_rows = lax.all_gather(compact, "head", axis=1, tiled=True)
    picked = jnp.take(full_rows, jnp.clip(order, 0, most - 1), axis=0)
    replaced = jnp.where(taken[:, None], picked, embeddings)
    arrived = lax.all_to_all(rotated_cache_pages, "tok", split_axis=1, concat_axis=0, tiled=True)
    page_size = arrived.shape[2]
    pages = arrived.reshape(members * page_size, -1)
    queries_two, keys_two, values_two = project(
        replaced, norm_gain, query_key_value_weight, positions
    )
    return attend_both(
        query_vectors, block_keys, block_values, queries_two, keys_two, values_two, pages, usable
    )


def solution(mesh):
    return jax.shard_map(
        body,
        mesh=mesh,
        in_specs=(
            P("tok", None),
            P(),
            P(None, "head"),
            P("tok", "head"),
            P("tok", None, None, "head"),
            P("tok", None),
            P("tok"),
            P("tok", None),
            P("tok"),
            P("tok"),
        ),
        out_specs=(P("tok", "head"), P("tok", "head")),
        check_vma=False,
    )
```

```python
import math

import jax
import jax.numpy as jnp
from jax import lax
from jax.experimental import pallas as pl
from jax.experimental.pallas import tpu as pltpu
from jax.sharding import PartitionSpec as P

QUERY_HEADS = 32
KEY_VALUE_HEADS = 8
HEAD_SIZE = 128
HEADS_PER_GROUP = QUERY_HEADS // KEY_VALUE_HEADS


THETA = 500000.0
KEY_CHUNK = 2048


def angles(positions):
    steps_half = jnp.arange(HEAD_SIZE // 2, dtype=jnp.float32)
    frequency = THETA ** (-(steps_half * 2.0) / HEAD_SIZE)
    return positions.astype(jnp.float32)[:, None] * frequency[None, :]


def rotate(vectors, turning):
    half_width = vectors.shape[-1] // 2
    former = vectors[..., :half_width]
    latter = vectors[..., half_width:]
    cosine = jnp.cos(turning)
    sine_of = jnp.sin(turning)
    return jnp.concatenate(
        [former * cosine - latter * sine_of, latter * cosine + former * sine_of], axis=-1
    )


def project(inputs, norm_gain, query_key_value_weight, positions):
    widened = inputs.astype(jnp.float32)
    inverse = lax.rsqrt(jnp.mean(widened * widened, axis=-1, keepdims=True) + 1e-05)
    normed = (widened * inverse * norm_gain.astype(jnp.float32)).astype(jnp.bfloat16)
    combined = jnp.dot(normed, query_key_value_weight, preferred_element_type=jnp.float32)
    rows = inputs.shape[0]
    combined = combined.reshape(rows, -1, HEADS_PER_GROUP + 2, HEAD_SIZE)
    turning = angles(positions)[:, None, None, :]
    query_vectors = rotate(combined[:, :, :HEADS_PER_GROUP], turning).astype(jnp.bfloat16)
    block_keys = rotate(combined[:, :, HEADS_PER_GROUP : HEADS_PER_GROUP + 1], turning)[
        :, :, 0
    ].astype(jnp.bfloat16)
    block_values = combined[:, :, HEADS_PER_GROUP + 1].astype(jnp.bfloat16)
    return (
        query_vectors.reshape(rows, -1),
        block_keys.reshape(rows, -1),
        block_values.reshape(rows, -1),
    )


def attention_kernel(q1_ref, q2_ref, kb1_ref, vb1_ref, kb2_ref, vb2_ref, pg_ref, us_ref,
                     o1_ref, o2_ref, s_ref):
    factor = 1.0 / math.sqrt(HEAD_SIZE)
    nt = (((1,), (1,)), ((), ()))
    rows = q1_ref.shape[0]
    q = jnp.concatenate([q1_ref[...], q2_ref[...]], axis=0)
    sb1 = lax.dot_general(q1_ref[...], kb1_ref[...], nt, preferred_element_type=jnp.float32) * factor
    sb2 = lax.dot_general(q2_ref[...], kb2_ref[...], nt, preferred_element_type=jnp.float32) * factor
    high = jnp.concatenate(
        [jnp.max(sb1, axis=1, keepdims=True), jnp.max(sb2, axis=1, keepdims=True)], axis=0
    )
    keys_total = pg_ref.shape[0]
    chunks = keys_total // KEY_CHUNK
    for c in range(chunks):
        lo = c * KEY_CHUNK
        k = pg_ref[lo : lo + KEY_CHUNK, 0:HEAD_SIZE]
        sc = lax.dot_general(q, k, nt, preferred_element_type=jnp.float32) * factor
        sc = jnp.where(us_ref[:, lo : lo + KEY_CHUNK] > 0, sc, -1e30)
        s_ref[:, lo : lo + KEY_CHUNK] = sc
        high = jnp.maximum(high, jnp.max(sc, axis=1, keepdims=True))
    h1 = high[:rows]
    h2 = high[rows:]
    eb1 = jnp.exp(sb1 - h1)
    eb2 = jnp.exp(sb2 - h2)
    tot = jnp.concatenate(
        [jnp.sum(eb1, axis=1, keepdims=True), jnp.sum(eb2, axis=1, keepdims=True)], axis=0
    )
    acc = jnp.concatenate(
        [
            jnp.dot(eb1.astype(jnp.bfloat16), vb1_ref[...], preferred_element_type=jnp.float32),
            jnp.dot(eb2.astype(jnp.bfloat16), vb2_ref[...], preferred_element_type=jnp.float32),
        ],
        axis=0,
    )
    for c in range(chunks):
        lo = c * KEY_CHUNK
        e = jnp.exp(s_ref[:, lo : lo + KEY_CHUNK] - high)
        tot = tot + jnp.sum(e, axis=1, keepdims=True)
        v = pg_ref[lo : lo + KEY_CHUNK, HEAD_SIZE : 2 * HEAD_SIZE]
        acc = acc + jnp.dot(e.astype(jnp.bfloat16), v, preferred_element_type=jnp.float32)
    res = (acc / tot).astype(jnp.bfloat16)
    o1_ref[...] = res[:rows]
    o2_ref[...] = res[rows:]


def attend_both(q1, kb1, vb1, q2, kb2, vb2, pages, usable):
    rows = q1.shape[0]
    keys_total = pages.shape[0]
    qspec = pl.BlockSpec((rows, HEAD_SIZE), lambda j: (0, j))
    full = pl.BlockSpec((rows, HEAD_SIZE), lambda j: (0, 0))
    return pl.pallas_call(
        attention_kernel,
        grid=(HEADS_PER_GROUP,),
        in_specs=[
            qspec,
            qspec,
            full,
            full,
            full,
            full,
            pl.BlockSpec((keys_total, 2 * HEAD_SIZE), lambda j: (0, 0)),
            pl.BlockSpec((1, keys_total), lambda j: (0, 0)),
        ],
        out_specs=[qspec, qspec],
        out_shape=[
            jax.ShapeDtypeStruct(q1.shape, jnp.bfloat16),
            jax.ShapeDtypeStruct(q1.shape, jnp.bfloat16),
        ],
        scratch_shapes=[pltpu.VMEM((2 * rows, keys_total), jnp.float32)],
        compiler_params=pltpu.CompilerParams(vmem_limit_bytes=48 * 1024 * 1024),
    )(q1, q2, kb1, vb1, kb2, vb2, pages, usable)


def body(
    embeddings,
    norm_gain,
    query_key_value_weight,
    embed_table,
    rotated_cache_pages,
    page_owner_device,
    cached_length,
    vocab_shard,
    shard_row,
    accept,
):
    members = lax.axis_size("tok")
    length = embeddings.shape[0]
    sources = jnp.arange(members, dtype=jnp.int32)
    positions = cached_length[0] + jnp.arange(length, dtype=jnp.int32)
    page_size = rotated_cache_pages.shape[2]
    page_index = jnp.sum(
        jnp.where(page_owner_device[0][:, None] == sources[None, :], sources[:, None], 0), axis=0
    )
    page_spots = page_index[:, None] * page_size + jnp.arange(page_size, dtype=jnp.int32)[None, :]
    usable = (page_spots.reshape(1, -1) < cached_length[0]).astype(jnp.float32)

    query_vectors, block_keys, block_values = project(
        embeddings, norm_gain, query_key_value_weight, positions
    )
    target_shard = vocab_shard[:, 0]
    capacity = max(2, 2 * length // members)
    chosen = (target_shard[:, None] == sources[None, :]).astype(jnp.int32)
    earlier = (jnp.arange(length)[:, None] > jnp.arange(length)[None, :]).astype(jnp.int32)
    slot_rank = jnp.sum(jnp.dot(earlier, chosen) * chosen, axis=1)
    slot_of = target_shard * capacity + slot_rank
    slots = jnp.arange(members * capacity, dtype=jnp.int32)
    wanted = jnp.sum(
        jnp.where(slot_of[:, None] == slots[None, :], shard_row[:, None], 0), axis=0
    ).reshape(members, capacity)
    asked = lax.all_to_all(wanted, "tok", split_axis=0, concat_axis=0, tiled=True)
    found_rows = jnp.take(embed_table, asked, axis=0)
    returned = lax.all_to_all(found_rows, "tok", split_axis=0, concat_axis=0, tiled=True)
    taken = accept == 1
    most = members
    order = jnp.cumsum(taken.astype(jnp.int32)) - 1
    slots = jnp.arange(most, dtype=jnp.int32)
    hit = taken[:, None] & (order[:, None] == slots[None, :])
    token_of = jnp.sum(jnp.where(hit, jnp.arange(length, dtype=jnp.int32)[:, None], 0), axis=0)
    compact = returned[target_shard[token_of], slot_rank[token_of]]
    full_rows = lax.all_gather(compact, "head", axis=1, tiled=True)
    picked = jnp.take(full_rows, jnp.clip(order, 0, most - 1), axis=0)
    replaced = jnp.where(taken[:, None], picked, embeddings)
    arrived = lax.all_to_all(rotated_cache_pages, "tok", split_axis=1, concat_axis=0, tiled=True)
    page_size = arrived.shape[2]
    pages = arrived.reshape(members * page_size, -1)
    queries_two, keys_two, values_two = project(
        replaced, norm_gain, query_key_value_weight, positions
    )
    return attend_both(
        query_vectors, block_keys, block_values, queries_two, keys_two, values_two, pages, usable
    )


def solution(mesh):
    return jax.shard_map(
        body,
        mesh=mesh,
        in_specs=(
            P("tok", None),
            P(),
            P(None, "head"),
            P("tok", "head"),
            P("tok", None, None, "head"),
            P("tok", None),
            P("tok"),
            P("tok", None),
            P("tok"),
            P("tok"),
        ),
        out_specs=(P("tok", "head"), P("tok", "head")),
        check_vma=False,
    )
```
